32 devices in a mesh: groups: 2 (over y), frames: 4 (over z), heads: 4 (over x, core).
Axes of the slice: x: 2, y: 2, z: 4, core: 2. Of those that a mesh axis runs over, the one named last changes fastest.
Arguments:
- query_heads: bfloat16 [16384, 896], P(('groups', 'frames'), 'heads'), parts along dimension 0, may hold values from -6 to 6
- key_heads: bfloat16 [16384, 896], P(('groups', 'frames'), 'heads'), parts along dimension 0, may hold values from -0.04 to 8
- value_heads: bfloat16 [16384, 896], P(('groups', 'frames'), 'heads'), parts along dimension 0, may hold values from -6 to 6
- residual: bfloat16 [16384, 2240], P(('groups', 'frames', 'heads')), parts along dimension 0, may hold values from -6 to 6
- out_proj: bfloat16 [896, 2240], P('frames'), may hold values from -0.1875 to 0.1875
- frame_gate: float32 [32, 2240], P(('groups', 'frames')), parts along dimension 0, may hold values from -4 to 4
Outputs:
- updated: bfloat16 [16384, 2240], P(('groups', 'frames', 'heads')), parts along dimension 0
The draws below stay inside these ranges and needn't reach their ends.
There are 2 independent parts, one for each index of `groups`. The reference program is written for one: setup_inputs(seed, part) draws one part's arguments, and reference() takes and returns one part's arrays. A program takes and returns all parts, laid end to end along the dimension named above; an argument that names none is the same for every part. Nothing has to cross between parts.
All inputs are finite; a program needn't handle non-finite values.
Results may differ from the reference program's by a relative error of at most 0.0033.
Values may be sent and summed in bfloat16 or wider, within the bound.
No kernel may reach another device: no remote copies, remote signals or barrier semaphores. Data moves between devices by JAX's collectives and lax.ppermute only.
A program may use at most 64 MiB of HBM per device.

```python
import math
import jax
import jax.numpy as jnp
from jax import lax

D = 2240
HD = 112
FRAME_TOK = 512
HEADS = 8
FRAMES = 16
TOKENS = 8192


def active_dims(key):
    frames_all = TOKENS // FRAME_TOK
    pick_key, base_key, offset_key, mixer_key = jax.random.split(jax.random.fold_in(key, 71), 4)
    anywhere = jax.random.randint(pick_key, (frames_all, FRAME_TOK, HEADS), 0, HD)
    window_base = jax.random.randint(base_key, (frames_all, 1, HEADS), 0, HD)
    window_step = jax.random.randint(offset_key, (frames_all, FRAME_TOK, HEADS), 0, max(HD // 3, 1))
    in_window = (window_base + window_step) % HD
    mixer = jax.random.randint(mixer_key, (frames_all, FRAME_TOK, HEADS), 0, 2)
    chosen = jnp.where(mixer == 0, anywhere, in_window)
    return chosen.reshape(TOKENS, HEADS).astype(jnp.int32)


def draw_key_heads(key, part):
    dims = active_dims(key)
    onehot = (dims[:, :, None] == jnp.arange(HD, dtype=jnp.int32)[None, None, :]).astype(jnp.float32)
    noise_key, amp_key = jax.random.split(jax.random.fold_in(key, 17))
    noise_part = jnp.clip(jax.random.normal(noise_key, (TOKENS, HEADS, HD), jnp.float32), -3.0, 3.0)
    log_amp = jax.random.uniform(amp_key, (TOKENS, HEADS, 1), jnp.float32, math.log(3.0), math.log(10.0))
    shaped = onehot * jnp.exp(log_amp) + 0.02 + 0.02 * noise_part
    return jnp.clip(shaped, -0.04, 8.0).reshape(TOKENS, HEADS * HD).astype(jnp.bfloat16)


def draw_value_heads(key, part):
    frames_all = TOKENS // FRAME_TOK
    dims = active_dims(key)
    table_key, noise_key, offset_key = jax.random.split(jax.random.fold_in(key, 29), 3)
    table = jnp.clip(jax.random.normal(table_key, (HEADS, HD, HD), jnp.float32), -3.0, 3.0)
    head_index = jnp.arange(HEADS, dtype=jnp.int32)[None, :]
    picked = table[head_index, dims]
    offsets = jnp.clip(jax.random.normal(offset_key, (frames_all, 1, HEADS, HD), jnp.float32), -3.0, 3.0)
    picked = picked.reshape(frames_all, FRAME_TOK, HEADS, HD)
    noise_part = jnp.clip(jax.random.normal(noise_key, (frames_all, FRAME_TOK, HEADS, HD), jnp.float32), -3.0, 3.0)
    shaped = 2.0 * picked + offsets + 0.4 * noise_part
    return jnp.clip(shaped, -6.0, 6.0).reshape(TOKENS, HEADS * HD).astype(jnp.bfloat16)


def level_of(own_key, extent, shards, smallest, top_value):
    def one(axis_at, shards_of):
        heights = jax.random.uniform(jax.random.fold_in(jax.random.fold_in(own_key, 6), axis_at), (shards_of,), jnp.float32, smallest / len(shards), top_value / len(shards))
        return jnp.repeat(jnp.exp(heights), extent[axis_at] // shards_of).reshape((-1,) + (1,) * (len(extent) - axis_at - 1))

    loudness = one(*shards[0])
    for cut in shards[1:]:
        loudness = loudness * one(*cut)
    return loudness


def bell_draw(stream_key, extent, spread, most, cuts=(), kind=jnp.bfloat16):
    drawn = jax.random.normal(stream_key, extent, jnp.float32) * spread
    if len(cuts) > 0:
        drawn = level_of(stream_key, extent, cuts, -0.22, 0.18) * drawn
    return jnp.clip(drawn, min=-most, max=most).astype(kind)


def setup_inputs(seed: int = 0, part: int = 0) -> dict:
    arg_keys = jax.random.split(jax.random.key(seed), 7)
    part_keys = jax.random.split(jax.random.fold_in(arg_keys[6], part), 7)
    return {
        "query_heads": bell_draw(part_keys[0], (TOKENS, HEADS * HD), 1.0, 6.0, ((0, 4), (1, 4))),
        "key_heads": draw_key_heads(jax.random.fold_in(jax.random.fold_in(arg_keys[6], part), 71), part),
        "value_heads": draw_value_heads(jax.random.fold_in(jax.random.fold_in(arg_keys[6], part), 71), part),
        "residual": bell_draw(part_keys[3], (TOKENS, D), 1.0, 6.0, ((0, 16),)),
        "out_proj": bell_draw(arg_keys[4], (HEADS * HD, D), (HEADS * HD) ** -0.5, 0.1875, ((0, 4),)),
        "frame_gate": bell_draw(part_keys[5], (FRAMES, D), 1.0, 4.0, ((0, 4),), jnp.float32),
    }


EPSILON = 1e-6


def reference(query_heads, key_heads, value_heads, residual, out_proj, frame_gate):
    frames_all = TOKENS // FRAME_TOK
    block_shape = (frames_all, FRAME_TOK, HEADS, HD)
    query_pos = jnp.maximum(query_heads, 0).reshape(block_shape)
    key_pos = jnp.maximum(key_heads, 0).reshape(block_shape)
    value_frames = value_heads.reshape(block_shape)

    def advance(carry, inputs):
        state_sum, key_total = carry
        query_frame, key_frame, value_frame = inputs
        key_wide = key_frame.astype(jnp.float32)
        state_sum = state_sum + jnp.einsum("thi,thj->hij", key_wide, value_frame.astype(jnp.float32))
        key_total = key_total + jnp.sum(key_wide, axis=0)
        state_round = lax.optimization_barrier(state_sum.astype(jnp.bfloat16)).astype(jnp.float32)
        sum_round = lax.optimization_barrier(key_total.astype(jnp.bfloat16)).astype(jnp.float32)
        query_wide = query_frame.astype(jnp.float32)
        numerator = jnp.einsum("thi,hij->thj", query_wide, state_round)
        denominator = jnp.einsum("thi,hi->th", query_wide, sum_round) + EPSILON
        attended = (numerator / denominator[:, :, None]).astype(jnp.bfloat16)
        return (state_sum, key_total), attended.reshape(FRAME_TOK, HEADS * HD)

    start_state = (jnp.zeros((HEADS, HD, HD), jnp.float32), jnp.zeros((HEADS, HD), jnp.float32))
    final_carry, attended = lax.scan(advance, start_state, (query_pos, key_pos, value_frames))
    attended = attended.reshape(TOKENS, HEADS * HD)
    projected = jnp.dot(attended, out_proj, preferred_element_type=jnp.float32)
    gate_rows = jnp.repeat(frame_gate, FRAME_TOK, axis=0)
    return (residual.astype(jnp.float32) + gate_rows * projected).astype(jnp.bfloat16)
```

```python
import jax
import jax.numpy as jnp
from jax import lax
from jax.sharding import PartitionSpec as P

HD = 112
FRAME_TOK = 512


EPSILON = 1e-06


def _exclusive_prefix(x, nf):
    if nf <= 8:
        total = jnp.zeros_like(x)
        for d in range(1, nf):
            total = total + lax.ppermute(x, "frames", [(i, i + d) for i in range(nf - d)])
        return total
    y = lax.ppermute(x, "frames", [(i, i + 1) for i in range(nf - 1)])
    covered = 1
    while covered < nf - 1:
        y = y + lax.ppermute(y, "frames", [(i, i + covered) for i in range(nf - covered)])
        covered *= 2
    return y


def _gather_out_proj(out_proj, nf, nh):
    rows, cols = out_proj.shape
    half = rows // 2
    j = lax.axis_index("frames")
    core = lax.axis_index("heads") % 2
    mine = lax.dynamic_slice_in_dim(out_proj, core * half, half, axis=0)
    swap = [(a, a ^ 1) for a in range(nh)]
    buf = jnp.zeros((nf, 2, half, cols), out_proj.dtype)
    buf = lax.dynamic_update_slice(buf, out_proj.reshape(1, 2, half, cols), (j, 0, 0, 0))
    left = mine
    right = mine
    for t in range(1, nf):
        left = lax.ppermute(left, "frames", [(i, i + 1) for i in range(t - 1, nf - 1)])
        right = lax.ppermute(right, "frames", [(i, i - 1) for i in range(1, nf - t + 1)])
        for piece, block in ((left, j - t), (right, j + t)):
            other = lax.ppermute(piece, "heads", swap)
            slot = jnp.remainder(block, nf)
            for part, side in ((piece, core), (other, 1 - core)):
                cur = lax.dynamic_slice(buf, (slot, side, 0, 0), (1, 1, half, cols))
                buf = lax.dynamic_update_slice(
                    buf, cur + part.reshape(1, 1, half, cols), (slot, side, 0, 0)
                )
    return buf.reshape(nf * rows, cols)


def make_per_device(nf, nh):
    def per_device(query_heads, key_heads, value_heads, residual, out_proj, frame_gate):
        length, width = query_heads.shape
        frames_here = length // FRAME_TOK
        heads_here = width // HD
        block_shape = (frames_here, FRAME_TOK, width)
        query_pos = jnp.maximum(query_heads, 0).reshape(block_shape)
        key_pos = jnp.maximum(key_heads, 0).reshape(block_shape)
        value_frames = value_heads.reshape(block_shape)
        lane_head = jnp.arange(width, dtype=jnp.int32) // HD
        same_head = lane_head[:, None] == lane_head[None, :]

        frame_state = jnp.einsum(
            "fti,ftj->fij", key_pos, value_frames, preferred_element_type=jnp.float32
        )
        frame_state = jnp.where(same_head[None], frame_state, 0.0)
        frame_sum = jnp.sum(key_pos, axis=1, dtype=jnp.float32)
        own_state = jnp.sum(frame_state, axis=0)
        own_sum = jnp.sum(frame_sum, axis=0)

        blocks = [
            own_state[a * HD:(a + 1) * HD, a * HD:(a + 1) * HD] for a in range(heads_here)
        ]
        compact = jnp.concatenate(
            [jnp.stack(blocks), own_sum.reshape(heads_here, 1, HD)], axis=1
        )
        earlier = _exclusive_prefix(compact, nf)
        eye = jnp.eye(heads_here, dtype=jnp.float32)
        earlier_state = jnp.einsum(
            "aij,ab->aibj", earlier[:, :HD, :], eye, precision=lax.Precision.HIGHEST
        ).reshape(width, width)
        earlier_sum = earlier[:, HD, :].reshape(width)

        prefix_state = earlier_state[None] + jnp.cumsum(frame_state, axis=0)
        prefix_sum = earlier_sum[None] + jnp.cumsum(frame_sum, axis=0)
        state_round = prefix_state.astype(jnp.bfloat16)
        sum_round = prefix_sum.astype(jnp.bfloat16)
        sum_matrix = jnp.where(same_head[None], sum_round[:, :, None], jnp.zeros((), jnp.bfloat16))
        numerator = jnp.einsum(
            "fti,fij->ftj", query_pos, state_round, preferred_element_type=jnp.float32
        )
        denominator = (
            jnp.einsum("fti,fij->ftj", query_pos, sum_matrix, preferred_element_type=jnp.float32)
            + EPSILON
        )
        attended = (numerator / denominator).astype(jnp.bfloat16).reshape(length, width)

        weights = _gather_out_proj(out_proj, nf, nh)

        rows_here = residual.shape[0]
        head_pos = lax.axis_index("heads")
        if rows_here <= FRAME_TOK and FRAME_TOK % rows_here == 0:
            gate_rows = lax.dynamic_slice_in_dim(
                frame_gate, (head_pos * rows_here) // FRAME_TOK, 1, axis=0
            )
        else:
            row_frame = (head_pos * rows_here + jnp.arange(rows_here, dtype=jnp.int32)) // FRAME_TOK
            gate_rows = jnp.take(frame_gate, row_frame, axis=0)
        token_rows = lax.all_to_all(attended, "heads", split_axis=0, concat_axis=1, tiled=True)
        projected = jnp.dot(token_rows, weights, preferred_element_type=jnp.float32)
        return (residual.astype(jnp.float32) + gate_rows * projected).astype(jnp.bfloat16)

    return per_device


def solution(mesh):
    nf = mesh.shape["frames"]
    nh = mesh.shape["heads"]
    in_specs = (
        P(("groups", "frames"), "heads"),
        P(("groups", "frames"), "heads"),
        P(("groups", "frames"), "heads"),
        P(("groups", "frames", "heads"), None),
        P("frames", None),
        P(("groups", "frames"), None),
    )
    out_specs = P(("groups", "frames", "heads"), None)
    return jax.shard_map(
        make_per_device(nf, nh), mesh=mesh, in_specs=in_specs, out_specs=out_specs, check_vma=False
    )
```

```python
import jax
import jax.numpy as jnp
from jax import lax
from jax.sharding import PartitionSpec as P

HD = 112
FRAME_TOK = 512


EPSILON = 1e-06


def _exclusive_prefix(x, nf):
    if nf <= 8:
        total = jnp.zeros_like(x)
        for d in range(1, nf):
            total = total + lax.ppermute(x, "frames", [(i, i + d) for i in range(nf - d)])
        return total
    y = lax.ppermute(x, "frames", [(i, i + 1) for i in range(nf - 1)])
    covered = 1
    while covered < nf - 1:
        y = y + lax.ppermute(y, "frames", [(i, i + covered) for i in range(nf - covered)])
        covered *= 2
    return y


def _ring_out_proj(out_proj, nf, nh):
    rows, cols = out_proj.shape
    half = rows // 2
    core = lax.axis_index("heads") % 2
    mine = lax.dynamic_slice_in_dim(out_proj, core * half, half, axis=0)
    theirs = lax.dynamic_slice_in_dim(out_proj, (1 - core) * half, half, axis=0)
    ring = [(i, (i + 1) % nf) for i in range(nf)]
    swap = [(a, a ^ 1) for a in range(nh)]
    mine_pieces = [mine]
    their_pieces = [theirs]
    piece = mine
    for _ in range(1, nf):
        piece = lax.ppermute(piece, "frames", ring)
        mine_pieces.append(piece)
        their_pieces.append(lax.ppermute(piece, "heads", swap))
    return jnp.stack(mine_pieces + their_pieces)


def make_per_device(nf, nh):
    def per_device(query_heads, key_heads, value_heads, residual, out_proj, frame_gate):
        length, width = query_heads.shape
        frames_here = length // FRAME_TOK
        heads_here = width // HD
        block_shape = (frames_here, FRAME_TOK, width)
        query_pos = jnp.maximum(query_heads, 0).reshape(block_shape)
        key_pos = jnp.maximum(key_heads, 0).reshape(block_shape)
        value_frames = value_heads.reshape(block_shape)
        lane_head = jnp.arange(width, dtype=jnp.int32) // HD
        same_head = lane_head[:, None] == lane_head[None, :]

        frame_state = jnp.einsum(
            "fti,ftj->fij", key_pos, value_frames, preferred_element_type=jnp.float32
        )
        frame_state = jnp.where(same_head[None], frame_state, 0.0)
        frame_sum = jnp.sum(key_pos, axis=1, dtype=jnp.float32)
        own_state = jnp.sum(frame_state, axis=0)
        own_sum = jnp.sum(frame_sum, axis=0)

        blocks = [
            own_state[a * HD:(a + 1) * HD, a * HD:(a + 1) * HD] for a in range(heads_here)
        ]
        compact = jnp.concatenate(
            [jnp.stack(blocks), own_sum.reshape(heads_here, 1, HD)], axis=1
        )
        earlier = _exclusive_prefix(compact, nf)
        eye = jnp.eye(heads_here, dtype=jnp.float32)
        earlier_state = jnp.einsum(
            "aij,ab->aibj", earlier[:, :HD, :], eye, precision=lax.Precision.HIGHEST
        ).reshape(width, width)
        earlier_sum = earlier[:, HD, :].reshape(width)

        prefix_state = earlier_state[None] + jnp.cumsum(frame_state, axis=0)
        prefix_sum = earlier_sum[None] + jnp.cumsum(frame_sum, axis=0)
        state_round = prefix_state.astype(jnp.bfloat16)
        sum_round = prefix_sum.astype(jnp.bfloat16)
        sum_matrix = jnp.where(same_head[None], sum_round[:, :, None], jnp.zeros((), jnp.bfloat16))
        numerator = jnp.einsum(
            "fti,fij->ftj", query_pos, state_round, preferred_element_type=jnp.float32
        )
        denominator = (
            jnp.einsum("fti,fij->ftj", query_pos, sum_matrix, preferred_element_type=jnp.float32)
            + EPSILON
        )
        attended = (numerator / denominator).astype(jnp.bfloat16).reshape(length, width)

        weights = _ring_out_proj(out_proj, nf, nh)

        rows_here = residual.shape[0]
        head_pos = lax.axis_index("heads")
        if rows_here <= FRAME_TOK and FRAME_TOK % rows_here == 0:
            gate_rows = lax.dynamic_slice_in_dim(
                frame_gate, (head_pos * rows_here) // FRAME_TOK, 1, axis=0
            )
        else:
            row_frame = (head_pos * rows_here + jnp.arange(rows_here, dtype=jnp.int32)) // FRAME_TOK
            gate_rows = jnp.take(frame_gate, row_frame, axis=0)
        token_rows = lax.all_to_all(attended, "heads", split_axis=0, concat_axis=1, tiled=True)
        rows_w, cols_w = out_proj.shape
        half = rows_w // 2
        by_half = token_rows.reshape(rows_here, nf * 2, half).transpose(1, 0, 2)
        j = lax.axis_index("frames")
        core = head_pos % 2
        block = jnp.remainder(j - jnp.arange(nf, dtype=jnp.int32), nf)
        order = jnp.concatenate([block * 2 + core, block * 2 + 1 - core])
        matched = jnp.take(by_half, order, axis=0)
        projected = jnp.einsum(
            "ktr,krc->tc", matched, weights, preferred_element_type=jnp.float32
        )
        return (residual.astype(jnp.float32) + gate_rows * projected).astype(jnp.bfloat16)

    return per_device


def solution(mesh):
    nf = mesh.shape["frames"]
    nh = mesh.shape["heads"]
    in_specs = (
        P(("groups", "frames"), "heads"),
        P(("groups", "frames"), "heads"),
        P(("groups", "frames"), "heads"),
        P(("groups", "frames", "heads"), None),
        P("frames", None),
        P(("groups", "frames"), None),
    )
    out_specs = P(("groups", "frames", "heads"), None)
    return jax.shard_map(
        make_per_device(nf, nh), mesh=mesh, in_specs=in_specs, out_specs=out_specs, check_vma=False
    )
```

```python
import jax
import jax.numpy as jnp
from jax import lax
from jax.sharding import PartitionSpec as P

HD = 112
FRAME_TOK = 512


EPSILON = 1e-06


def _exclusive_prefix(x, nf):
    if nf <= 8:
        total = jnp.zeros_like(x)
        for d in range(1, nf):
            total = total + lax.ppermute(x, "frames", [(i, i + d) for i in range(nf - d)])
        return total
    y = lax.ppermute(x, "frames", [(i, i + 1) for i in range(nf - 1)])
    covered = 1
    while covered < nf - 1:
        y = y + lax.ppermute(y, "frames", [(i, i + covered) for i in range(nf - covered)])
        covered *= 2
    return y


def _ring_out_proj(out_proj, nf, nh, ng):
    rows, _ = out_proj.shape
    sub = rows // (2 * ng)
    g = lax.axis_index("groups")
    core = lax.axis_index("heads") % 2
    shares = [jnp.remainder(g - s, ng) * 2 + core for s in range(ng)]
    shares += [jnp.remainder(g - s, ng) * 2 + 1 - core for s in range(ng)]
    pieces = [lax.dynamic_slice_in_dim(out_proj, share * sub, sub, axis=0) for share in shares]
    swap = [(a, a ^ 1) for a in range(nh)]
    fetched = []
    for t in range(1, nf):
        fetched.append(lax.ppermute(pieces[0], "frames", [(i, (i + t) % nf) for i in range(nf)]))
    fetched = jnp.stack(fetched)
    from_groups = [fetched] + [
        lax.ppermute(fetched, "groups", [(a, (a + s) % ng) for a in range(ng)])
        for s in range(1, ng)
    ]
    mine = jnp.stack(from_groups, axis=1)
    theirs = lax.ppermute(mine, "heads", swap)
    for t in range(nf - 1):
        pieces += [mine[t, s] for s in range(ng)] + [theirs[t, s] for s in range(ng)]
    return jnp.concatenate(pieces, axis=0), jnp.stack(shares)


def make_per_device(nf, nh, ng):
    def per_device(query_heads, key_heads, value_heads, residual, out_proj, frame_gate):
        weights, shares = _ring_out_proj(out_proj, nf, nh, ng)
        attended = _attend(query_heads, key_heads, value_heads, nf)
        return _project(attended, weights, shares, residual, frame_gate, nf, ng)

    return per_device


def _attend(query_heads, key_heads, value_heads, nf):
    length, width = query_heads.shape
    frames_here = length // FRAME_TOK
    heads_here = width // HD
    block_shape = (frames_here, FRAME_TOK, width)
    query_pos = jnp.maximum(query_heads, 0).reshape(block_shape)
    key_pos = jnp.maximum(key_heads, 0).reshape(block_shape)
    value_frames = value_heads.reshape(block_shape)
    lane_head = jnp.arange(width, dtype=jnp.int32) // HD
    same_head = lane_head[:, None] == lane_head[None, :]

    frame_state = jnp.einsum(
        "fti,ftj->fij", key_pos, value_frames, preferred_element_type=jnp.float32
    )
    frame_state = jnp.where(same_head[None], frame_state, 0.0)
    frame_sum = jnp.sum(key_pos, axis=1, dtype=jnp.float32)
    own_state = jnp.sum(frame_state, axis=0)
    own_sum = jnp.sum(frame_sum, axis=0)

    blocks = [
        own_state[a * HD:(a + 1) * HD, a * HD:(a + 1) * HD] for a in range(heads_here)
    ]
    compact = jnp.concatenate(
        [jnp.stack(blocks), own_sum.reshape(heads_here, 1, HD)], axis=1
    )
    earlier = _exclusive_prefix(compact, nf)
    eye = jnp.eye(heads_here, dtype=jnp.float32)
    earlier_state = jnp.einsum(
        "aij,ab->aibj", earlier[:, :HD, :], eye, precision=lax.Precision.HIGHEST
    ).reshape(width, width)
    earlier_sum = earlier[:, HD, :].reshape(width)

    prefix_state = earlier_state[None] + jnp.cumsum(frame_state, axis=0)
    prefix_sum = earlier_sum[None] + jnp.cumsum(frame_sum, axis=0)
    state_round = prefix_state.astype(jnp.bfloat16)
    sum_round = prefix_sum.astype(jnp.bfloat16)
    sum_matrix = jnp.where(same_head[None], sum_round[:, :, None], jnp.zeros((), jnp.bfloat16))
    numerator = jnp.einsum(
        "fti,fij->ftj", query_pos, state_round, preferred_element_type=jnp.float32
    )
    denominator = (
        jnp.einsum("fti,fij->ftj", query_pos, sum_matrix, preferred_element_type=jnp.float32)
        + EPSILON
    )
    return (numerator / denominator).astype(jnp.bfloat16).reshape(length, width)


def _project(attended, weights, shares, residual, frame_gate, nf, ng):
    rows_here = residual.shape[0]
    head_pos = lax.axis_index("heads")
    if rows_here <= FRAME_TOK and FRAME_TOK % rows_here == 0:
        gate_rows = lax.dynamic_slice_in_dim(
            frame_gate, (head_pos * rows_here) // FRAME_TOK, 1, axis=0
        )
    else:
        row_frame = (head_pos * rows_here + jnp.arange(rows_here, dtype=jnp.int32)) // FRAME_TOK
        gate_rows = jnp.take(frame_gate, row_frame, axis=0)
    token_rows = lax.all_to_all(attended, "heads", split_axis=0, concat_axis=1, tiled=True)
    nparts = 2 * ng
    depth = weights.shape[0]
    sub = depth // (nf * nparts)
    j = lax.axis_index("frames")
    block = jnp.remainder(j - jnp.arange(nf, dtype=jnp.int32), nf)
    order = (block[:, None] * nparts + shares[None, :]).reshape(-1)
    source = (order[:, None] * sub + jnp.arange(sub, dtype=jnp.int32)[None, :]).reshape(-1)
    pick = (jnp.arange(depth, dtype=jnp.int32)[:, None] == source[None, :]).astype(jnp.bfloat16)
    matched = jnp.dot(token_rows, pick, preferred_element_type=jnp.float32).astype(jnp.bfloat16)
    projected = jnp.dot(matched, weights, preferred_element_type=jnp.float32)
    return (residual.astype(jnp.float32) + gate_rows * projected).astype(jnp.bfloat16)


def solution(mesh):
    nf = mesh.shape["frames"]
    nh = mesh.shape["heads"]
    ng = mesh.shape["groups"]
    in_specs = (
        P(("groups", "frames"), "heads"),
        P(("groups", "frames"), "heads"),
        P(("groups", "frames"), "heads"),
        P(("groups", "frames", "heads"), None),
        P("frames", None),
        P(("groups", "frames"), None),
    )
    out_specs = P(("groups", "frames", "heads"), None)
    return jax.shard_map(
        make_per_device(nf, nh, ng), mesh=mesh, in_specs=in_specs, out_specs=out_specs,
        check_vma=False,
    )
```

```python
import jax
import jax.numpy as jnp
from jax import lax
from jax.sharding import PartitionSpec as P

HD = 112
FRAME_TOK = 512


EPSILON = 1e-06


def _exclusive_prefix(x, nf):
    if nf <= 8:
        total = jnp.zeros_like(x)
        for d in range(1, nf):
            total = total + lax.ppermute(x, "frames", [(i, i + d) for i in range(nf - d)])
        return total
    y = lax.ppermute(x, "frames", [(i, i + 1) for i in range(nf - 1)])
    covered = 1
    while covered < nf - 1:
        y = y + lax.ppermute(y, "frames", [(i, i + covered) for i in range(nf - covered)])
        covered *= 2
    return y


def _gather_out_proj(out_proj, nf, nh, ng):
    rows, cols = out_proj.shape
    sub = rows // (2 * ng)
    g = lax.axis_index("groups")
    core = lax.axis_index("heads") % 2
    mine = lax.dynamic_slice_in_dim(out_proj, (2 * g + core) * sub, sub, axis=0)
    gathered = lax.all_gather(mine, ("groups", "frames"), axis=0)
    theirs = lax.ppermute(gathered, "heads", [(a, a ^ 1) for a in range(nh)])
    weights = jnp.concatenate([gathered, theirs], axis=0).reshape(2 * ng * nf * sub, cols)
    group_of = jnp.repeat(jnp.arange(ng, dtype=jnp.int32), nf)
    block = jnp.tile(jnp.arange(nf, dtype=jnp.int32), 2 * ng)
    share = jnp.concatenate([2 * group_of + core, 2 * group_of + 1 - core])
    return weights, block, share


def make_per_device(nf, nh, ng):
    def per_device(query_heads, key_heads, value_heads, residual, out_proj, frame_gate):
        weights, block, share = _gather_out_proj(out_proj, nf, nh, ng)
        attended = _attend(query_heads, key_heads, value_heads, nf)
        return _project(attended, weights, block, share, residual, frame_gate, nf, ng)

    return per_device


def _attend(query_heads, key_heads, value_heads, nf):
    length, width = query_heads.shape
    frames_here = length // FRAME_TOK
    heads_here = width // HD
    block_shape = (frames_here, FRAME_TOK, width)
    query_pos = jnp.maximum(query_heads, 0).reshape(block_shape)
    key_pos = jnp.maximum(key_heads, 0).reshape(block_shape)
    value_frames = value_heads.reshape(block_shape)
    lane_head = jnp.arange(width, dtype=jnp.int32) // HD
    same_head = lane_head[:, None] == lane_head[None, :]

    frame_state = jnp.einsum(
        "fti,ftj->fij", key_pos, value_frames, preferred_element_type=jnp.float32
    )
    frame_state = jnp.where(same_head[None], frame_state, 0.0)
    frame_sum = jnp.sum(key_pos, axis=1, dtype=jnp.float32)
    own_state = jnp.sum(frame_state, axis=0)
    own_sum = jnp.sum(frame_sum, axis=0)

    blocks = [
        own_state[a * HD:(a + 1) * HD, a * HD:(a + 1) * HD] for a in range(heads_here)
    ]
    compact = jnp.concatenate(
        [jnp.stack(blocks), own_sum.reshape(heads_here, 1, HD)], axis=1
    )
    earlier = _exclusive_prefix(compact, nf)
    eye = jnp.eye(heads_here, dtype=jnp.float32)
    earlier_state = jnp.einsum(
        "aij,ab->aibj", earlier[:, :HD, :], eye, precision=lax.Precision.HIGHEST
    ).reshape(width, width)
    earlier_sum = earlier[:, HD, :].reshape(width)

    prefix_state = earlier_state[None] + jnp.cumsum(frame_state, axis=0)
    prefix_sum = earlier_sum[None] + jnp.cumsum(frame_sum, axis=0)
    state_round = prefix_state.astype(jnp.bfloat16)
    sum_round = prefix_sum.astype(jnp.bfloat16)
    sum_matrix = jnp.where(same_head[None], sum_round[:, :, None], jnp.zeros((), jnp.bfloat16))
    numerator = jnp.einsum(
        "fti,fij->ftj", query_pos, state_round, preferred_element_type=jnp.float32
    )
    denominator = (
        jnp.einsum("fti,fij->ftj", query_pos, sum_matrix, preferred_element_type=jnp.float32)
        + EPSILON
    )
    return (numerator / denominator).astype(jnp.bfloat16).reshape(length, width)


def _project(attended, weights, block, share, residual, frame_gate, nf, ng):
    rows_here = residual.shape[0]
    head_pos = lax.axis_index("heads")
    if rows_here <= FRAME_TOK and FRAME_TOK % rows_here == 0:
        gate_rows = lax.dynamic_slice_in_dim(
            frame_gate, (head_pos * rows_here) // FRAME_TOK, 1, axis=0
        )
    else:
        row_frame = (head_pos * rows_here + jnp.arange(rows_here, dtype=jnp.int32)) // FRAME_TOK
        gate_rows = jnp.take(frame_gate, row_frame, axis=0)
    token_rows = lax.all_to_all(attended, "heads", split_axis=0, concat_axis=1, tiled=True)
    depth = weights.shape[0]
    sub = depth // (nf * 2 * ng)
    row_of = (block * (2 * ng) + share) * sub
    source = (row_of[:, None] + jnp.arange(sub, dtype=jnp.int32)[None, :]).reshape(-1)
    pick = (jnp.arange(depth, dtype=jnp.int32)[:, None] == source[None, :]).astype(jnp.bfloat16)
    matched = jnp.dot(token_rows, pick, preferred_element_type=jnp.float32).astype(jnp.bfloat16)
    projected = jnp.dot(matched, weights, preferred_element_type=jnp.float32)
    return (residual.astype(jnp.float32) + gate_rows * projected).astype(jnp.bfloat16)


def solution(mesh):
    nf = mesh.shape["frames"]
    nh = mesh.shape["heads"]
    ng = mesh.shape["groups"]
    in_specs = (
        P(("groups", "frames"), "heads"),
        P(("groups", "frames"), "heads"),
        P(("groups", "frames"), "heads"),
        P(("groups", "frames", "heads"), None),
        P("frames", None),
        P(("groups", "frames"), None),
    )
    out_specs = P(("groups", "frames", "heads"), None)
    return jax.shard_map(
        make_per_device(nf, nh, ng), mesh=mesh, in_specs=in_specs, out_specs=out_specs,
        check_vma=False,
    )
```

```python
import jax
import jax.numpy as jnp
from jax import lax
from jax.sharding import PartitionSpec as P

HD = 112
FRAME_TOK = 512


EPSILON = 1e-06


def _exclusive_prefix(x, nf):
    if nf <= 8:
        total = jnp.zeros_like(x)
        for d in range(1, nf):
            total = total + lax.ppermute(x, "frames", [(i, i + d) for i in range(nf - d)])
        return total
    y = lax.ppermute(x, "frames", [(i, i + 1) for i in range(nf - 1)])
    covered = 1
    while covered < nf - 1:
        y = y + lax.ppermute(y, "frames", [(i, i + covered) for i in range(nf - covered)])
        covered *= 2
    return y


def _ring_out_proj(out_proj, nf, nh, ng):
    rows, _ = out_proj.shape
    sub = rows // (2 * ng)
    g = lax.axis_index("groups")
    core = lax.axis_index("heads") % 2
    shares = [jnp.remainder(g - s, ng) * 2 + core for s in range(ng)]
    shares += [jnp.remainder(g - s, ng) * 2 + 1 - core for s in range(ng)]
    pieces = [lax.dynamic_slice_in_dim(out_proj, share * sub, sub, axis=0) for share in shares]
    ring = [(i, (i + 1) % nf) for i in range(nf)]
    swap = [(a, a ^ 1) for a in range(nh)]
    piece = pieces[0]
    for _ in range(1, nf):
        piece = lax.ppermute(piece, "frames", ring)
        from_groups = [piece] + [
            lax.ppermute(piece, "groups", [(a, (a + s) % ng) for a in range(ng)])
            for s in range(1, ng)
        ]
        from_core = lax.ppermute(jnp.stack(from_groups), "heads", swap)
        pieces += from_groups + [from_core[s] for s in range(ng)]
    return jnp.concatenate(pieces, axis=0), jnp.stack(shares)


def make_per_device(nf, nh, ng):
    def per_device(query_heads, key_heads, value_heads, residual, out_proj, frame_gate):
        weights, shares = _ring_out_proj(out_proj, nf, nh, ng)
        attended = _attend(query_heads, key_heads, value_heads, nf)
        return _project(attended, weights, shares, residual, frame_gate, nf, ng)

    return per_device


def _attend(query_heads, key_heads, value_heads, nf):
    length, width = query_heads.shape
    frames_here = length // FRAME_TOK
    heads_here = width // HD
    block_shape = (frames_here, FRAME_TOK, width)
    query_pos = jnp.maximum(query_heads, 0).reshape(block_shape)
    key_pos = jnp.maximum(key_heads, 0).reshape(block_shape)
    value_frames = value_heads.reshape(block_shape)
    lane_head = jnp.arange(width, dtype=jnp.int32) // HD
    same_head = lane_head[:, None] == lane_head[None, :]

    frame_state = jnp.einsum(
        "fti,ftj->fij", key_pos, value_frames, preferred_element_type=jnp.float32
    )
    frame_state = jnp.where(same_head[None], frame_state, 0.0)
    frame_sum = jnp.sum(key_pos, axis=1, dtype=jnp.float32)
    own_state = jnp.sum(frame_state, axis=0)
    own_sum = jnp.sum(frame_sum, axis=0)

    blocks = [
        own_state[a * HD:(a + 1) * HD, a * HD:(a + 1) * HD] for a in range(heads_here)
    ]
    compact = jnp.concatenate(
        [jnp.stack(blocks), own_sum.reshape(heads_here, 1, HD)], axis=1
    )
    earlier = _exclusive_prefix(compact, nf)
    eye = jnp.eye(heads_here, dtype=jnp.float32)
    earlier_state = jnp.einsum(
        "aij,ab->aibj", earlier[:, :HD, :], eye, precision=lax.Precision.HIGHEST
    ).reshape(width, width)
    earlier_sum = earlier[:, HD, :].reshape(width)

    prefix_state = earlier_state[None] + jnp.cumsum(frame_state, axis=0)
    prefix_sum = earlier_sum[None] + jnp.cumsum(frame_sum, axis=0)
    state_round = prefix_state.astype(jnp.bfloat16)
    sum_round = prefix_sum.astype(jnp.bfloat16)
    sum_matrix = jnp.where(same_head[None], sum_round[:, :, None], jnp.zeros((), jnp.bfloat16))
    numerator = jnp.einsum(
        "fti,fij->ftj", query_pos, state_round, preferred_element_type=jnp.float32
    )
    denominator = (
        jnp.einsum("fti,fij->ftj", query_pos, sum_matrix, preferred_element_type=jnp.float32)
        + EPSILON
    )
    return (numerator / denominator).astype(jnp.bfloat16).reshape(length, width)


def _project(attended, weights, shares, residual, frame_gate, nf, ng):
    rows_here = residual.shape[0]
    head_pos = lax.axis_index("heads")
    if rows_here <= FRAME_TOK and FRAME_TOK % rows_here == 0:
        gate_rows = lax.dynamic_slice_in_dim(
            frame_gate, (head_pos * rows_here) // FRAME_TOK, 1, axis=0
        )
    else:
        row_frame = (head_pos * rows_here + jnp.arange(rows_here, dtype=jnp.int32)) // FRAME_TOK
        gate_rows = jnp.take(frame_gate, row_frame, axis=0)
    token_rows = lax.all_to_all(attended, "heads", split_axis=0, concat_axis=1, tiled=True)
    nparts = 2 * ng
    depth = weights.shape[0]
    sub = depth // (nf * nparts)
    j = lax.axis_index("frames")
    block = jnp.remainder(j - jnp.arange(nf, dtype=jnp.int32), nf)
    order = (block[:, None] * nparts + shares[None, :]).reshape(-1)
    source = (order[:, None] * sub + jnp.arange(sub, dtype=jnp.int32)[None, :]).reshape(-1)
    pick = (jnp.arange(depth, dtype=jnp.int32)[:, None] == source[None, :]).astype(jnp.bfloat16)
    matched = jnp.dot(token_rows, pick, preferred_element_type=jnp.float32).astype(jnp.bfloat16)
    projected = jnp.dot(matched, weights, preferred_element_type=jnp.float32)
    return (residual.astype(jnp.float32) + gate_rows * projected).astype(jnp.bfloat16)


def solution(mesh):
    nf = mesh.shape["frames"]
    nh = mesh.shape["heads"]
    ng = mesh.shape["groups"]
    in_specs = (
        P(("groups", "frames"), "heads"),
        P(("groups", "frames"), "heads"),
        P(("groups", "frames"), "heads"),
        P(("groups", "frames", "heads"), None),
        P("frames", None),
        P(("groups", "frames"), None),
    )
    out_specs = P(("groups", "frames", "heads"), None)
    return jax.shard_map(
        make_per_device(nf, nh, ng), mesh=mesh, in_specs=in_specs, out_specs=out_specs,
        check_vma=False,
    )
```

```python
import jax
import jax.numpy as jnp
from jax import lax
from jax.sharding import PartitionSpec as P

HD = 112
FRAME_TOK = 512


EPSILON = 1e-06


def _exclusive_prefix(x, nf):
    if nf <= 8:
        total = jnp.zeros_like(x)
        for d in range(1, nf):
            total = total + lax.ppermute(x, "frames", [(i, i + d) for i in range(nf - d)])
        return total
    y = lax.ppermute(x, "frames", [(i, i + 1) for i in range(nf - 1)])
    covered = 1
    while covered < nf - 1:
        y = y + lax.ppermute(y, "frames", [(i, i + covered) for i in range(nf - covered)])
        covered *= 2
    return y


def _ring_out_proj(out_proj, nf, nh, ng):
    rows, _ = out_proj.shape
    sub = rows // (2 * ng)
    g = lax.axis_index("groups")
    core = lax.axis_index("heads") % 2
    shares = [jnp.remainder(g - s, ng) * 2 + core for s in range(ng)]
    shares += [jnp.remainder(g - s, ng) * 2 + 1 - core for s in range(ng)]
    pieces = [lax.dynamic_slice_in_dim(out_proj, share * sub, sub, axis=0) for share in shares]
    forward = [(i, (i + 1) % nf) for i in range(nf)]
    backward = [(i, (i - 1) % nf) for i in range(nf)]
    swap = [(a, a ^ 1) for a in range(nh)]
    offsets = [0]

    def spread(piece):
        from_groups = [piece] + [
            lax.ppermute(piece, "groups", [(a, (a + s) % ng) for a in range(ng)])
            for s in range(1, ng)
        ]
        from_core = lax.ppermute(jnp.stack(from_groups), "heads", swap)
        return from_groups + [from_core[s] for s in range(ng)]

    ahead = nf // 2
    behind = nf - 1 - ahead
    piece_a = pieces[0]
    piece_b = pieces[0]
    for t in range(1, ahead + 1):
        piece_a = lax.ppermute(piece_a, "frames", forward)
        if t <= behind:
            piece_b = lax.ppermute(piece_b, "frames", backward)
        pieces += spread(piece_a)
        offsets.append(-t)
        if t <= behind:
            pieces += spread(piece_b)
            offsets.append(t)
    return jnp.concatenate(pieces, axis=0), jnp.stack(shares), offsets


def make_per_device(nf, nh, ng):
    def per_device(query_heads, key_heads, value_heads, residual, out_proj, frame_gate):
        weights, shares, offsets = _ring_out_proj(out_proj, nf, nh, ng)
        attended = _attend(query_heads, key_heads, value_heads, nf)
        return _project(attended, weights, shares, offsets, residual, frame_gate, nf, ng)

    return per_device


def _attend(query_heads, key_heads, value_heads, nf):
    length, width = query_heads.shape
    frames_here = length // FRAME_TOK
    heads_here = width // HD
    block_shape = (frames_here, FRAME_TOK, width)
    query_pos = jnp.maximum(query_heads, 0).reshape(block_shape)
    key_pos = jnp.maximum(key_heads, 0).reshape(block_shape)
    value_frames = value_heads.reshape(block_shape)
    lane_head = jnp.arange(width, dtype=jnp.int32) // HD
    same_head = lane_head[:, None] == lane_head[None, :]

    frame_state = jnp.einsum(
        "fti,ftj->fij", key_pos, value_frames, preferred_element_type=jnp.float32
    )
    frame_state = jnp.where(same_head[None], frame_state, 0.0)
    frame_sum = jnp.sum(key_pos, axis=1, dtype=jnp.float32)
    own_state = jnp.sum(frame_state, axis=0)
    own_sum = jnp.sum(frame_sum, axis=0)

    blocks = [
        own_state[a * HD:(a + 1) * HD, a * HD:(a + 1) * HD] for a in range(heads_here)
    ]
    compact = jnp.concatenate(
        [jnp.stack(blocks), own_sum.reshape(heads_here, 1, HD)], axis=1
    )
    earlier = _exclusive_prefix(compact, nf)
    eye = jnp.eye(heads_here, dtype=jnp.float32)
    earlier_state = jnp.einsum(
        "aij,ab->aibj", earlier[:, :HD, :], eye, precision=lax.Precision.HIGHEST
    ).reshape(width, width)
    earlier_sum = earlier[:, HD, :].reshape(width)

    prefix_state = earlier_state[None] + jnp.cumsum(frame_state, axis=0)
    prefix_sum = earlier_sum[None] + jnp.cumsum(frame_sum, axis=0)
    state_round = prefix_state.astype(jnp.bfloat16)
    sum_round = prefix_sum.astype(jnp.bfloat16)
    sum_matrix = jnp.where(same_head[None], sum_round[:, :, None], jnp.zeros((), jnp.bfloat16))
    numerator = jnp.einsum(
        "fti,fij->ftj", query_pos, state_round, preferred_element_type=jnp.float32
    )
    denominator = (
        jnp.einsum("fti,fij->ftj", query_pos, sum_matrix, preferred_element_type=jnp.float32)
        + EPSILON
    )
    return (numerator / denominator).astype(jnp.bfloat16).reshape(length, width)


def _project(attended, weights, shares, offsets, residual, frame_gate, nf, ng):
    rows_here = residual.shape[0]
    head_pos = lax.axis_index("heads")
    if rows_here <= FRAME_TOK and FRAME_TOK % rows_here == 0:
        gate_rows = lax.dynamic_slice_in_dim(
            frame_gate, (head_pos * rows_here) // FRAME_TOK, 1, axis=0
        )
    else:
        row_frame = (head_pos * rows_here + jnp.arange(rows_here, dtype=jnp.int32)) // FRAME_TOK
        gate_rows = jnp.take(frame_gate, row_frame, axis=0)
    token_rows = lax.all_to_all(attended, "heads", split_axis=0, concat_axis=1, tiled=True)
    nparts = 2 * ng
    depth = weights.shape[0]
    sub = depth // (nf * nparts)
    j = lax.axis_index("frames")
    block = jnp.remainder(j + jnp.array(offsets, dtype=jnp.int32), nf)
    order = (block[:, None] * nparts + shares[None, :]).reshape(-1)
    source = (order[:, None] * sub + jnp.arange(sub, dtype=jnp.int32)[None, :]).reshape(-1)
    pick = (jnp.arange(depth, dtype=jnp.int32)[:, None] == source[None, :]).astype(jnp.bfloat16)
    matched = jnp.dot(token_rows, pick, preferred_element_type=jnp.float32).astype(jnp.bfloat16)
    projected = jnp.dot(matched, weights, preferred_element_type=jnp.float32)
    return (residual.astype(jnp.float32) + gate_rows * projected).astype(jnp.bfloat16)


def solution(mesh):
    nf = mesh.shape["frames"]
    nh = mesh.shape["heads"]
    ng = mesh.shape["groups"]
    in_specs = (
        P(("groups", "frames"), "heads"),
        P(("groups", "frames"), "heads"),
        P(("groups", "frames"), "heads"),
        P(("groups", "frames", "heads"), None),
        P("frames", None),
        P(("groups", "frames"), None),
    )
    out_specs = P(("groups", "frames", "heads"), None)
    return jax.shard_map(
        make_per_device(nf, nh, ng), mesh=mesh, in_specs=in_specs, out_specs=out_specs,
        check_vma=False,
    )
```

```python
import jax
import jax.numpy as jnp
from jax import lax
from jax.sharding import PartitionSpec as P

HD = 112
FRAME_TOK = 512


EPSILON = 1e-06


def _exclusive_prefix(x, nf):
    i = lax.axis_index("frames")
    later = jnp.arange(nf, dtype=jnp.int32) > i
    outgoing = jnp.where(
        later.reshape((nf,) + (1,) * x.ndim), jnp.broadcast_to(x, (nf,) + x.shape), 0.0
    )
    incoming = lax.all_to_all(outgoing, "frames", split_axis=0, concat_axis=0, tiled=True)
    return jnp.sum(incoming, axis=0)


def _ring_out_proj(out_proj, nf, nh, ng):
    rows, _ = out_proj.shape
    sub = rows // (2 * ng)
    g = lax.axis_index("groups")
    core = lax.axis_index("heads") % 2
    shares = [jnp.remainder(g - s, ng) * 2 + core for s in range(ng)]
    shares += [jnp.remainder(g - s, ng) * 2 + 1 - core for s in range(ng)]
    pieces = [lax.dynamic_slice_in_dim(out_proj, share * sub, sub, axis=0) for share in shares]
    ring = [(i, (i + 1) % nf) for i in range(nf)]
    swap = [(a, a ^ 1) for a in range(nh)]
    piece = pieces[0]
    for _ in range(1, nf):
        piece = lax.ppermute(piece, "frames", ring)
        from_groups = [piece] + [
            lax.ppermute(piece, "groups", [(a, (a + s) % ng) for a in range(ng)])
            for s in range(1, ng)
        ]
        from_core = lax.ppermute(jnp.stack(from_groups), "heads", swap)
        pieces += from_groups + [from_core[s] for s in range(ng)]
    return jnp.concatenate(pieces, axis=0), jnp.stack(shares)


def make_per_device(nf, nh, ng):
    def per_device(query_heads, key_heads, value_heads, residual, out_proj, frame_gate):
        weights, shares = _ring_out_proj(out_proj, nf, nh, ng)
        attended = _attend(query_heads, key_heads, value_heads, nf)
        return _project(attended, weights, shares, residual, frame_gate, nf, ng)

    return per_device


def _attend(query_heads, key_heads, value_heads, nf):
    length, width = query_heads.shape
    frames_here = length // FRAME_TOK
    heads_here = width // HD
    block_shape = (frames_here, FRAME_TOK, width)
    query_pos = jnp.maximum(query_heads, 0).reshape(block_shape)
    key_pos = jnp.maximum(key_heads, 0).reshape(block_shape)
    value_frames = value_heads.reshape(block_shape)
    lane_head = jnp.arange(width, dtype=jnp.int32) // HD
    same_head = lane_head[:, None] == lane_head[None, :]

    frame_state = jnp.einsum(
        "fti,ftj->fij", key_pos, value_frames, preferred_element_type=jnp.float32
    )
    frame_state = jnp.where(same_head[None], frame_state, 0.0)
    frame_sum = jnp.sum(key_pos, axis=1, dtype=jnp.float32)
    own_state = jnp.sum(frame_state, axis=0)
    own_sum = jnp.sum(frame_sum, axis=0)

    blocks = [
        own_state[a * HD:(a + 1) * HD, a * HD:(a + 1) * HD] for a in range(heads_here)
    ]
    compact = jnp.concatenate(
        [jnp.stack(blocks), own_sum.reshape(heads_here, 1, HD)], axis=1
    )
    earlier = _exclusive_prefix(compact, nf)
    eye = jnp.eye(heads_here, dtype=jnp.float32)
    earlier_state = jnp.einsum(
        "aij,ab->aibj", earlier[:, :HD, :], eye, precision=lax.Precision.HIGHEST
    ).reshape(width, width)
    earlier_sum = earlier[:, HD, :].reshape(width)

    prefix_state = earlier_state[None] + jnp.cumsum(frame_state, axis=0)
    prefix_sum = earlier_sum[None] + jnp.cumsum(frame_sum, axis=0)
    state_round = prefix_state.astype(jnp.bfloat16)
    sum_round = prefix_sum.astype(jnp.bfloat16)
    sum_matrix = jnp.where(same_head[None], sum_round[:, :, None], jnp.zeros((), jnp.bfloat16))
    numerator = jnp.einsum(
        "fti,fij->ftj", query_pos, state_round, preferred_element_type=jnp.float32
    )
    denominator = (
        jnp.einsum("fti,fij->ftj", query_pos, sum_matrix, preferred_element_type=jnp.float32)
        + EPSILON
    )
    return (numerator / denominator).astype(jnp.bfloat16).reshape(length, width)


def _project(attended, weights, shares, residual, frame_gate, nf, ng):
    rows_here = residual.shape[0]
    head_pos = lax.axis_index("heads")
    if rows_here <= FRAME_TOK and FRAME_TOK % rows_here == 0:
        gate_rows = lax.dynamic_slice_in_dim(
            frame_gate, (head_pos * rows_here) // FRAME_TOK, 1, axis=0
        )
    else:
        row_frame = (head_pos * rows_here + jnp.arange(rows_here, dtype=jnp.int32)) // FRAME_TOK
        gate_rows = jnp.take(frame_gate, row_frame, axis=0)
    token_rows = lax.all_to_all(attended, "heads", split_axis=0, concat_axis=1, tiled=True)
    nparts = 2 * ng
    depth = weights.shape[0]
    sub = depth // (nf * nparts)
    j = lax.axis_index("frames")
    block = jnp.remainder(j - jnp.arange(nf, dtype=jnp.int32), nf)
    order = (block[:, None] * nparts + shares[None, :]).reshape(-1)
    source = (order[:, None] * sub + jnp.arange(sub, dtype=jnp.int32)[None, :]).reshape(-1)
    pick = (jnp.arange(depth, dtype=jnp.int32)[:, None] == source[None, :]).astype(jnp.bfloat16)
    matched = jnp.dot(token_rows, pick, preferred_element_type=jnp.float32).astype(jnp.bfloat16)
    projected = jnp.dot(matched, weights, preferred_element_type=jnp.float32)
    return (residual.astype(jnp.float32) + gate_rows * projected).astype(jnp.bfloat16)


def solution(mesh):
    nf = mesh.shape["frames"]
    nh = mesh.shape["heads"]
    ng = mesh.shape["groups"]
    in_specs = (
        P(("groups", "frames"), "heads"),
        P(("groups", "frames"), "heads"),
        P(("groups", "frames"), "heads"),
        P(("groups", "frames", "heads"), None),
        P("frames", None),
        P(("groups", "frames"), None),
    )
    out_specs = P(("groups", "frames", "heads"), None)
    return jax.shard_map(
        make_per_device(nf, nh, ng), mesh=mesh, in_specs=in_specs, out_specs=out_specs,
        check_vma=False,
    )
```

```python
import jax
import jax.numpy as jnp
from jax import lax
from jax.sharding import PartitionSpec as P

HD = 112
FRAME_TOK = 512


EPSILON = 1e-06


def _exclusive_prefix(x, nf):
    i = lax.axis_index("frames")
    later = jnp.arange(nf, dtype=jnp.int32) > i
    outgoing = jnp.where(
        later.reshape((nf,) + (1,) * x.ndim), jnp.broadcast_to(x, (nf,) + x.shape), 0.0
    )
    incoming = lax.all_to_all(outgoing, "frames", split_axis=0, concat_axis=0, tiled=True)
    return jnp.sum(incoming, axis=0)


def _ring_out_proj(out_proj, nf, nh, ng):
    rows, _ = out_proj.shape
    sub = rows // (2 * ng)
    g = lax.axis_index("groups")
    core = lax.axis_index("heads") % 2
    shares = [jnp.remainder(g - s, ng) * 2 + core for s in range(ng)]
    shares += [jnp.remainder(g - s, ng) * 2 + 1 - core for s in range(ng)]
    pieces = [lax.dynamic_slice_in_dim(out_proj, share * sub, sub, axis=0) for share in shares]
    forward = [(i, (i + 1) % nf) for i in range(nf)]
    backward = [(i, (i - 1) % nf) for i in range(nf)]
    swap = [(a, a ^ 1) for a in range(nh)]
    ahead = nf - 2 if nf >= 3 else nf - 1
    offsets = [0] + [-t for t in range(1, ahead + 1)]
    direct = None
    if ahead < nf - 1:
        direct = lax.ppermute(jnp.stack(pieces[:ng]), "frames", backward)
        offsets.append(1)
    piece = pieces[0]
    for _ in range(1, ahead + 1):
        piece = lax.ppermute(piece, "frames", forward)
        from_groups = [piece] + [
            lax.ppermute(piece, "groups", [(a, (a + s) % ng) for a in range(ng)])
            for s in range(1, ng)
        ]
        from_core = lax.ppermute(jnp.stack(from_groups), "heads", swap)
        pieces += from_groups + [from_core[s] for s in range(ng)]
    if direct is not None:
        direct_core = lax.ppermute(direct, "heads", swap)
        pieces += [direct[s] for s in range(ng)] + [direct_core[s] for s in range(ng)]
    return jnp.concatenate(pieces, axis=0), jnp.stack(shares), offsets


def make_per_device(nf, nh, ng):
    def per_device(query_heads, key_heads, value_heads, residual, out_proj, frame_gate):
        weights, shares, offsets = _ring_out_proj(out_proj, nf, nh, ng)
        attended = _attend(query_heads, key_heads, value_heads, nf)
        return _project(attended, weights, shares, offsets, residual, frame_gate, nf, ng)

    return per_device


def _attend(query_heads, key_heads, value_heads, nf):
    length, width = query_heads.shape
    frames_here = length // FRAME_TOK
    heads_here = width // HD
    block_shape = (frames_here, FRAME_TOK, width)
    query_pos = jnp.maximum(query_heads, 0).reshape(block_shape)
    key_pos = jnp.maximum(key_heads, 0).reshape(block_shape)
    value_frames = value_heads.reshape(block_shape)
    lane_head = jnp.arange(width, dtype=jnp.int32) // HD
    same_head = lane_head[:, None] == lane_head[None, :]

    frame_state = jnp.einsum(
        "fti,ftj->fij", key_pos, value_frames, preferred_element_type=jnp.float32
    )
    frame_state = jnp.where(same_head[None], frame_state, 0.0)
    frame_sum = jnp.sum(key_pos, axis=1, dtype=jnp.float32)
    own_state = jnp.sum(frame_state, axis=0)
    own_sum = jnp.sum(frame_sum, axis=0)

    blocks = [
        own_state[a * HD:(a + 1) * HD, a * HD:(a + 1) * HD] for a in range(heads_here)
    ]
    compact = jnp.concatenate(
        [jnp.stack(blocks), own_sum.reshape(heads_here, 1, HD)], axis=1
    )
    earlier = _exclusive_prefix(compact, nf)
    eye = jnp.eye(heads_here, dtype=jnp.float32)
    earlier_state = jnp.einsum(
        "aij,ab->aibj", earlier[:, :HD, :], eye, precision=lax.Precision.HIGHEST
    ).reshape(width, width)
    earlier_sum = earlier[:, HD, :].reshape(width)

    prefix_state = earlier_state[None] + jnp.cumsum(frame_state, axis=0)
    prefix_sum = earlier_sum[None] + jnp.cumsum(frame_sum, axis=0)
    state_round = prefix_state.astype(jnp.bfloat16)
    sum_round = prefix_sum.astype(jnp.bfloat16)
    sum_matrix = jnp.where(same_head[None], sum_round[:, :, None], jnp.zeros((), jnp.bfloat16))
    numerator = jnp.einsum(
        "fti,fij->ftj", query_pos, state_round, preferred_element_type=jnp.float32
    )
    denominator = (
        jnp.einsum("fti,fij->ftj", query_pos, sum_matrix, preferred_element_type=jnp.float32)
        + EPSILON
    )
    return (numerator / denominator).astype(jnp.bfloat16).reshape(length, width)


def _project(attended, weights, shares, offsets, residual, frame_gate, nf, ng):
    rows_here = residual.shape[0]
    head_pos = lax.axis_index("heads")
    if rows_here <= FRAME_TOK and FRAME_TOK % rows_here == 0:
        gate_rows = lax.dynamic_slice_in_dim(
            frame_gate, (head_pos * rows_here) // FRAME_TOK, 1, axis=0
        )
    else:
        row_frame = (head_pos * rows_here + jnp.arange(rows_here, dtype=jnp.int32)) // FRAME_TOK
        gate_rows = jnp.take(frame_gate, row_frame, axis=0)
    token_rows = lax.all_to_all(attended, "heads", split_axis=0, concat_axis=1, tiled=True)
    nparts = 2 * ng
    depth = weights.shape[0]
    sub = depth // (nf * nparts)
    j = lax.axis_index("frames")
    block = jnp.remainder(j + jnp.array(offsets, dtype=jnp.int32), nf)
    order = (block[:, None] * nparts + shares[None, :]).reshape(-1)
    source = (order[:, None] * sub + jnp.arange(sub, dtype=jnp.int32)[None, :]).reshape(-1)
    pick = (jnp.arange(depth, dtype=jnp.int32)[:, None] == source[None, :]).astype(jnp.bfloat16)
    matched = jnp.dot(token_rows, pick, preferred_element_type=jnp.float32).astype(jnp.bfloat16)
    projected = jnp.dot(matched, weights, preferred_element_type=jnp.float32)
    return (residual.astype(jnp.float32) + gate_rows * projected).astype(jnp.bfloat16)


def solution(mesh):
    nf = mesh.shape["frames"]
    nh = mesh.shape["heads"]
    ng = mesh.shape["groups"]
    in_specs = (
        P(("groups", "frames"), "heads"),
        P(("groups", "frames"), "heads"),
        P(("groups", "frames"), "heads"),
        P(("groups", "frames", "heads"), None),
        P("frames", None),
        P(("groups", "frames"), None),
    )
    out_specs = P(("groups", "frames", "heads"), None)
    return jax.shard_map(
        make_per_device(nf, nh, ng), mesh=mesh, in_specs=in_specs, out_specs=out_specs,
        check_vma=False,
    )
```

```python
import jax
import jax.numpy as jnp
from jax import lax
from jax.sharding import PartitionSpec as P

HD = 112
FRAME_TOK = 512


EPSILON = 1e-06


def _exclusive_prefix(x, nf):
    i = lax.axis_index("frames")
    later = jnp.arange(nf, dtype=jnp.int32) > i
    outgoing = jnp.where(
        later.reshape((nf,) + (1,) * x.ndim), jnp.broadcast_to(x, (nf,) + x.shape), 0.0
    )
    incoming = lax.all_to_all(outgoing, "frames", split_axis=0, concat_axis=0, tiled=True)
    return jnp.sum(incoming, axis=0)


def _ring_out_proj(out_proj, nf, nh, ng):
    rows, _ = out_proj.shape
    sub = rows // (2 * ng)
    g = lax.axis_index("groups")
    core = lax.axis_index("heads") % 2
    shares = [jnp.remainder(g - s, ng) * 2 + core for s in range(ng)]
    shares += [jnp.remainder(g - s, ng) * 2 + 1 - core for s in range(ng)]
    pieces = [lax.dynamic_slice_in_dim(out_proj, share * sub, sub, axis=0) for share in shares]
    ring = [(i, (i + 1) % nf) for i in range(nf)]
    swap = [(a, a ^ 1) for a in range(nh)]
    piece = pieces[0]
    for _ in range(1, nf):
        piece = lax.ppermute(piece, "frames", ring)
        from_groups = [piece] + [
            lax.ppermute(piece, "groups", [(a, (a + s) % ng) for a in range(ng)])
            for s in range(1, ng)
        ]
        from_core = lax.ppermute(jnp.stack(from_groups), "heads", swap)
        pieces += from_groups + [from_core[s] for s in range(ng)]
    return jnp.concatenate(pieces, axis=0), jnp.stack(shares)


def make_per_device(nf, nh, ng):
    def per_device(query_heads, key_heads, value_heads, residual, out_proj, frame_gate):
        weights, shares = _ring_out_proj(out_proj, nf, nh, ng)
        attended = _attend(query_heads, key_heads, value_heads, nf)
        return _project(attended, weights, shares, residual, frame_gate, nf, ng)

    return per_device


def _attend(query_heads, key_heads, value_heads, nf):
    length, width = query_heads.shape
    frames_here = length // FRAME_TOK
    heads_here = width // HD
    block_shape = (frames_here, FRAME_TOK, width)
    query_pos = jnp.maximum(query_heads, 0).reshape(block_shape)
    key_pos = jnp.maximum(key_heads, 0).reshape(block_shape)
    value_frames = value_heads.reshape(block_shape)
    lane_head = jnp.arange(width, dtype=jnp.int32) // HD
    same_head = lane_head[:, None] == lane_head[None, :]

    frame_state = jnp.einsum(
        "fti,ftj->fij", key_pos, value_frames, preferred_element_type=jnp.float32
    )
    frame_state = jnp.where(same_head[None], frame_state, 0.0)
    frame_sum = jnp.sum(key_pos, axis=1, dtype=jnp.float32)
    own_state = jnp.sum(frame_state, axis=0)
    own_sum = jnp.sum(frame_sum, axis=0)

    blocks = [
        own_state[a * HD:(a + 1) * HD, a * HD:(a + 1) * HD] for a in range(heads_here)
    ]
    compact = jnp.concatenate(
        [jnp.stack(blocks), own_sum.reshape(heads_here, 1, HD)], axis=1
    )
    earlier = _exclusive_prefix(compact, nf)
    eye = jnp.eye(heads_here, dtype=jnp.float32)
    earlier_state = jnp.einsum(
        "aij,ab->aibj", earlier[:, :HD, :], eye, precision=lax.Precision.HIGHEST
    ).reshape(width, width)
    earlier_sum = earlier[:, HD, :].reshape(width)

    prefix_state = earlier_state[None] + jnp.cumsum(frame_state, axis=0)
    prefix_sum = earlier_sum[None] + jnp.cumsum(frame_sum, axis=0)
    state_round = prefix_state.astype(jnp.bfloat16)
    sum_round = prefix_sum.astype(jnp.bfloat16)
    sum_matrix = jnp.where(same_head[None], sum_round[:, :, None], jnp.zeros((), jnp.bfloat16))
    numerator = jnp.einsum(
        "fti,fij->ftj", query_pos, state_round, preferred_element_type=jnp.float32
    )
    denominator = (
        jnp.einsum("fti,fij->ftj", query_pos, sum_matrix, preferred_element_type=jnp.float32)
        + EPSILON
    )
    return (numerator / denominator).astype(jnp.bfloat16).reshape(length, width)


def _project(attended, weights, shares, residual, frame_gate, nf, ng):
    rows_here = residual.shape[0]
    head_pos = lax.axis_index("heads")
    if rows_here <= FRAME_TOK and FRAME_TOK % rows_here == 0:
        gate_rows = lax.dynamic_slice_in_dim(
            frame_gate, (head_pos * rows_here) // FRAME_TOK, 1, axis=0
        )
    else:
        row_frame = (head_pos * rows_here + jnp.arange(rows_here, dtype=jnp.int32)) // FRAME_TOK
        gate_rows = jnp.take(frame_gate, row_frame, axis=0)
    token_rows = lax.all_to_all(attended, "heads", split_axis=0, concat_axis=1, tiled=True)
    nparts = 2 * ng
    depth = weights.shape[0]
    sub = depth // (nf * nparts)
    j = lax.axis_index("frames")
    block = jnp.remainder(j - jnp.arange(nf, dtype=jnp.int32), nf)
    order = (block[:, None] * nparts + shares[None, :]).reshape(-1)
    source = (order[:, None] * sub + jnp.arange(sub, dtype=jnp.int32)[None, :]).reshape(-1)
    columns = jnp.arange(depth, dtype=jnp.int32)[:, None]
    split = (nf - 1) * nparts * sub

    def part(lo, hi):
        pick = (columns == source[None, lo:hi]).astype(jnp.bfloat16)
        matched = jnp.dot(token_rows, pick, preferred_element_type=jnp.float32).astype(jnp.bfloat16)
        return jnp.dot(matched, weights[lo:hi], preferred_element_type=jnp.float32)

    projected = part(0, split) + part(split, depth)
    return (residual.astype(jnp.float32) + gate_rows * projected).astype(jnp.bfloat16)


def solution(mesh):
    nf = mesh.shape["frames"]
    nh = mesh.shape["heads"]
    ng = mesh.shape["groups"]
    in_specs = (
        P(("groups", "frames"), "heads"),
        P(("groups", "frames"), "heads"),
        P(("groups", "frames"), "heads"),
        P(("groups", "frames", "heads"), None),
        P("frames", None),
        P(("groups", "frames"), None),
    )
    out_specs = P(("groups", "frames", "heads"), None)
    return jax.shard_map(
        make_per_device(nf, nh, ng), mesh=mesh, in_specs=in_specs, out_specs=out_specs,
        check_vma=False,
    )
```

```python
import jax
import jax.numpy as jnp
from jax import lax
from jax.sharding import PartitionSpec as P

HD = 112
FRAME_TOK = 512


EPSILON = 1e-06


def _exclusive_prefix(x, nf):
    i = lax.axis_index("frames")
    later = jnp.arange(nf, dtype=jnp.int32) > i
    outgoing = jnp.where(
        later.reshape((nf,) + (1,) * x.ndim), jnp.broadcast_to(x, (nf,) + x.shape), 0.0
    )
    incoming = lax.all_to_all(outgoing, "frames", split_axis=0, concat_axis=0, tiled=True)
    return jnp.sum(incoming, axis=0)


def _ring_out_proj(out_proj, nf, nh, ng):
    rows, _ = out_proj.shape
    sub = rows // (2 * ng)
    g = lax.axis_index("groups")
    core = lax.axis_index("heads") % 2
    shares = [jnp.remainder(g - s, ng) * 2 + core for s in range(ng)]
    shares += [jnp.remainder(g - s, ng) * 2 + 1 - core for s in range(ng)]
    pieces = [lax.dynamic_slice_in_dim(out_proj, share * sub, sub, axis=0) for share in shares]
    ring = [(i, (i + 1) % nf) for i in range(nf)]
    swap = [(a, a ^ 1) for a in range(nh)]
    piece = pieces[0]
    for _ in range(1, nf):
        piece = lax.ppermute(piece, "frames", ring)
        from_groups = [piece] + [
            lax.ppermute(piece, "groups", [(a, (a + s) % ng) for a in range(ng)])
            for s in range(1, ng)
        ]
        from_core = [lax.ppermute(piece, "heads", swap)]
        if ng > 1:
            rest = lax.ppermute(jnp.stack(from_groups[1:]), "heads", swap)
            from_core += [rest[s] for s in range(ng - 1)]
        pieces += from_groups + from_core
    return jnp.concatenate(pieces, axis=0), jnp.stack(shares)


def make_per_device(nf, nh, ng):
    def per_device(query_heads, key_heads, value_heads, residual, out_proj, frame_gate):
        weights, shares = _ring_out_proj(out_proj, nf, nh, ng)
        attended = _attend(query_heads, key_heads, value_heads, nf)
        return _project(attended, weights, shares, residual, frame_gate, nf, ng)

    return per_device


def _attend(query_heads, key_heads, value_heads, nf):
    length, width = query_heads.shape
    frames_here = length // FRAME_TOK
    heads_here = width // HD
    block_shape = (frames_here, FRAME_TOK, width)
    query_pos = jnp.maximum(query_heads, 0).reshape(block_shape)
    key_pos = jnp.maximum(key_heads, 0).reshape(block_shape)
    value_frames = value_heads.reshape(block_shape)
    lane_head = jnp.arange(width, dtype=jnp.int32) // HD
    same_head = lane_head[:, None] == lane_head[None, :]

    frame_state = jnp.einsum(
        "fti,ftj->fij", key_pos, value_frames, preferred_element_type=jnp.float32
    )
    frame_state = jnp.where(same_head[None], frame_state, 0.0)
    frame_sum = jnp.sum(key_pos, axis=1, dtype=jnp.float32)
    own_state = jnp.sum(frame_state, axis=0)
    own_sum = jnp.sum(frame_sum, axis=0)

    blocks = [
        own_state[a * HD:(a + 1) * HD, a * HD:(a + 1) * HD] for a in range(heads_here)
    ]
    compact = jnp.concatenate(
        [jnp.stack(blocks), own_sum.reshape(heads_here, 1, HD)], axis=1
    )
    earlier = _exclusive_prefix(compact, nf)
    eye = jnp.eye(heads_here, dtype=jnp.float32)
    earlier_state = jnp.einsum(
        "aij,ab->aibj", earlier[:, :HD, :], eye, precision=lax.Precision.HIGHEST
    ).reshape(width, width)
    earlier_sum = earlier[:, HD, :].reshape(width)

    prefix_state = earlier_state[None] + jnp.cumsum(frame_state, axis=0)
    prefix_sum = earlier_sum[None] + jnp.cumsum(frame_sum, axis=0)
    state_round = prefix_state.astype(jnp.bfloat16)
    sum_round = prefix_sum.astype(jnp.bfloat16)
    sum_matrix = jnp.where(same_head[None], sum_round[:, :, None], jnp.zeros((), jnp.bfloat16))
    numerator = jnp.einsum(
        "fti,fij->ftj", query_pos, state_round, preferred_element_type=jnp.float32
    )
    denominator = (
        jnp.einsum("fti,fij->ftj", query_pos, sum_matrix, preferred_element_type=jnp.float32)
        + EPSILON
    )
    return (numerator / denominator).astype(jnp.bfloat16).reshape(length, width)


def _project(attended, weights, shares, residual, frame_gate, nf, ng):
    rows_here = residual.shape[0]
    head_pos = lax.axis_index("heads")
    if rows_here <= FRAME_TOK and FRAME_TOK % rows_here == 0:
        gate_rows = lax.dynamic_slice_in_dim(
            frame_gate, (head_pos * rows_here) // FRAME_TOK, 1, axis=0
        )
    else:
        row_frame = (head_pos * rows_here + jnp.arange(rows_here, dtype=jnp.int32)) // FRAME_TOK
        gate_rows = jnp.take(frame_gate, row_frame, axis=0)
    token_rows = lax.all_to_all(attended, "heads", split_axis=0, concat_axis=1, tiled=True)
    nparts = 2 * ng
    depth = weights.shape[0]
    sub = depth // (nf * nparts)
    j = lax.axis_index("frames")
    block = jnp.remainder(j - jnp.arange(nf, dtype=jnp.int32), nf)
    order = (block[:, None] * nparts + shares[None, :]).reshape(-1)
    source = (order[:, None] * sub + jnp.arange(sub, dtype=jnp.int32)[None, :]).reshape(-1)
    pick = (jnp.arange(depth, dtype=jnp.int32)[:, None] == source[None, :]).astype(jnp.bfloat16)
    matched = jnp.dot(token_rows, pick, preferred_element_type=jnp.float32).astype(jnp.bfloat16)
    projected = jnp.dot(matched, weights, preferred_element_type=jnp.float32)
    return (residual.astype(jnp.float32) + gate_rows * projected).astype(jnp.bfloat16)


def solution(mesh):
    nf = mesh.shape["frames"]
    nh = mesh.shape["heads"]
    ng = mesh.shape["groups"]
    in_specs = (
        P(("groups", "frames"), "heads"),
        P(("groups", "frames"), "heads"),
        P(("groups", "frames"), "heads"),
        P(("groups", "frames", "heads"), None),
        P("frames", None),
        P(("groups", "frames"), None),
    )
    out_specs = P(("groups", "frames", "heads"), None)
    return jax.shard_map(
        make_per_device(nf, nh, ng), mesh=mesh, in_specs=in_specs, out_specs=out_specs,
        check_vma=False,
    )
```
